128 devices in a mesh: pipe: 32 (over x, z, y_hi), dp: 4 (over y_lo, core).
Axes of the slice: x: 4, y: 4 (y_hi: 2, y_lo: 2; y = y_hi * 2 + y_lo), z: 4, core: 2. Of those that a mesh axis runs over, the one named last changes fastest.
Arguments:
- parked: bfloat16 [32, 8, 128, 8192], P('pipe', 'dp'), may hold values from -160 to 160
- slot_order: int32 [32, 4, 2], P('pipe', 'dp'), may hold values from 0 to 1, each once within a row
- segment_ids: int32 [32, 8, 128], P('pipe', 'dp'), may hold values from 0 to 3, never falling along the last dimension, each value on 1 to 64 neighbouring positions
- queries: bfloat16 [32, 8, 128, 4096], P('pipe', 'dp'), may hold values from -17 to 17
- out_grad: bfloat16 [32, 8, 128, 4096], P('pipe', 'dp'), may hold values from -4 to 4
- norm_gain: bfloat16 [32, 8192], P('pipe'), may hold values from 0.5 to 1.5
- kv_weight: bfloat16 [32, 8192, 1024], P('pipe', 'dp'), may hold values from -0.0625 to 0.0625
Outputs:
- upstream_grad: bfloat16 [32, 8, 128, 8192], P('pipe', 'dp')
- kv_weight_grad: bfloat16 [32, 8192, 1024], P('pipe', 'dp')
- gain_grad: float32 [32, 8192], P('pipe')
The draws below stay inside these ranges and needn't reach their ends.
All inputs are finite; a program needn't handle non-finite values.
Results may differ from the reference program's by a relative error of at most 0.012.
The reference program's roundings to bfloat16 on the way count: a program that leaves them out, or rounds other values in their place, can miss the bound.
Values may be sent and summed in bfloat16 or wider, within the bound.
No kernel may reach another device: no remote copies, remote signals or barrier semaphores. Data moves between devices by JAX's collectives and lax.ppermute only.
A program may use at most 128 MiB of HBM per device.

```python
import math
import jax
import jax.numpy as jnp
import numpy as np
from jax import lax

D = 8192
QH = 32
KVH = 4
HD = 128
S = 128
MB = 2
SECTIONS = 32
REPLICAS = 4
BATCH = 8
KVW = 1024
QW = 4096


def draw_parked(key, part):
    keys = jax.random.split(key, 3)
    shape = (SECTIONS, BATCH, S, D)
    row_scale = jnp.exp(jax.random.uniform(keys[1], (SECTIONS, BATCH, S, 1), jnp.float32, math.log(0.3), math.log(3.0)))
    col_scale = jnp.exp(jax.random.uniform(keys[2], (SECTIONS, 1, 1, D), jnp.float32, math.log(0.5), math.log(5.0)))
    noise = jax.random.truncated_normal(keys[0], -6.0, 6.0, shape, jnp.float32)
    values = row_scale * col_scale * noise
    return values.astype(jnp.bfloat16)


def draw_queries(key, part):
    keys = jax.random.split(key, 1)
    shape = (SECTIONS, BATCH, S, QW)
    values = jax.random.truncated_normal(keys[0], -6.0, 6.0, shape, jnp.float32)
    return values.astype(jnp.bfloat16)


def shard_levels(stream_key, extent, pieces, smallest, largest):
    level, own = 1.0, jax.random.fold_in(stream_key, 6)
    for axis_at, blocks in pieces:
        steps = jnp.exp(jax.random.uniform(jax.random.fold_in(own, axis_at), (blocks,), jnp.float32, smallest / len(pieces), largest / len(pieces)))
        level = level * jnp.repeat(steps, extent[axis_at] // blocks).reshape([-1 if axis == axis_at else 1 for axis in range(len(extent))])
    return level


def profile(amount, total, limit, lean):
    weights = [(1 << 20) // math.isqrt(grade ** lean) + 1 for grade in range(2, amount + 1)]
    rest, holding = total - limit - (amount - 1), [1] * (amount - 1)
    while rest > 0:
        free = [i for i in range(amount - 1) if holding[i] < limit]
        pool, budget = sum([weights[i] for i in free]), rest
        for i in free:
            more = min(limit - holding[i], max(1, budget * weights[i] // pool), rest)
            holding[i] = holding[i] + more
            rest = rest - more
    return np.array([limit] + holding)


def ragged_sizes(rng, count, total, reach, slope):
    if count == 2:
        one = jax.random.randint(rng, (), max(1, total - reach), min(reach, total - 1) + 1)
        return jnp.stack([one, total - one])
    sizes = jnp.asarray(profile(count, total, reach, slope), jnp.int32)
    couples = (count - 1) // 2
    donor, sink = sizes[1:1 + 2 * couples:2], sizes[2:2 + 2 * couples:2]
    margin = jnp.minimum(donor - 1, reach - sink)
    moved = jax.random.randint(jax.random.fold_in(rng, 1), (couples,), 0, 1 << 20) % (margin + 1)
    sizes = sizes.at[1:1 + 2 * couples:2].set(donor - moved).at[2:2 + 2 * couples:2].set(sink + moved)
    return sizes[jax.random.permutation(jax.random.fold_in(rng, 2), count)]


def normal_values(rng, dims, deviation, bound, cuts=(), kind=jnp.bfloat16):
    values = jax.random.normal(rng, dims, jnp.float32) * deviation
    if len(cuts) > 0:
        values = shard_levels(rng, dims, cuts, -0.22, 0.18) * values
    return jnp.clip(values, min=-bound, max=bound).astype(kind)


def setup_inputs(seed: int = 0) -> dict:
    splits = jax.random.split(jax.random.key(seed), 8)
    return {
        "parked": draw_parked(jax.random.fold_in(splits[7], 71), 0),
        "slot_order": jax.vmap(lambda own: jax.random.permutation(own, MB))(jax.random.split(splits[1], SECTIONS * REPLICAS)).reshape((SECTIONS, REPLICAS, MB)).astype(jnp.int32),
        "segment_ids": jax.vmap(lambda own: jnp.searchsorted(jnp.cumsum(ragged_sizes(own, 4, S, S // 2, 1)), jnp.arange(S), side="right"))(jax.random.split(splits[2], SECTIONS * BATCH)).reshape((SECTIONS, BATCH, S)).astype(jnp.int32),
        "queries": draw_queries(jax.random.fold_in(splits[7], 71), 0),
        "out_grad": normal_values(splits[4], (SECTIONS, BATCH, S, QW), 0.25, 4.0, ((0, 32), (1, 4))),
        "norm_gain": jnp.clip(1.0 + 0.1 * jax.random.normal(splits[5], (SECTIONS, D), jnp.float32), 0.5, 1.5).astype(jnp.bfloat16),
        "kv_weight": normal_values(splits[6], (SECTIONS, D, KVW), D ** -0.5, 0.0625, ((0, 32), (1, 4))),
    }


EPSILON = 1e-05

def attention_grads(queries, out_grad, keys, values, segments):
    batch_count = queries.shape[0]
    seq_len = queries.shape[1]
    group_size = QH // KVH
    scaling = 1.0 / math.sqrt(HD)
    query_heads = queries.astype(jnp.float32).reshape(batch_count, seq_len, KVH, group_size, HD)
    grad_heads = out_grad.astype(jnp.float32).reshape(batch_count, seq_len, KVH, group_size, HD)
    key_heads = keys.astype(jnp.float32).reshape(batch_count, seq_len, KVH, HD)
    value_heads = values.astype(jnp.float32).reshape(batch_count, seq_len, KVH, HD)
    scores = jnp.einsum('bqhgd,bkhd->bhgqk', query_heads, key_heads) * scaling
    position = jnp.arange(seq_len)
    causal = position[None, :] <= position[:, None]
    allowed = causal[None] & (segments[:, :, None] == segments[:, None, :])
    scores = jnp.where(allowed[:, None, None], scores, -1e+30)
    highest = lax.optimization_barrier(jnp.max(scores, axis=-1, keepdims=True))
    weights = jnp.exp(scores - highest)
    probabilities = weights / lax.optimization_barrier(jnp.sum(weights, axis=-1, keepdims=True))
    probs_low = probabilities.astype(jnp.bfloat16)
    value_grad = jnp.einsum('bhgqk,bqhgd->bkhd', probs_low.astype(jnp.float32), grad_heads)
    prob_grad = jnp.einsum('bqhgd,bkhd->bhgqk', grad_heads, value_heads)
    row_dot = lax.optimization_barrier(jnp.sum(probabilities * prob_grad, axis=-1, keepdims=True))
    score_grad = (probabilities * (prob_grad - row_dot) * scaling).astype(jnp.bfloat16)
    key_grad = jnp.einsum('bhgqk,bqhgd->bkhd', score_grad.astype(jnp.float32), query_heads)
    key_low = key_grad.astype(jnp.bfloat16).reshape(batch_count, seq_len, KVH * HD)
    value_low = value_grad.astype(jnp.bfloat16).reshape(batch_count, seq_len, KVH * HD)
    return jnp.concatenate([key_low, value_low], axis=-1)

def reference(parked, slot_order, segment_ids, queries, out_grad, norm_gain, kv_weight):

    def one_section(section_index):
        source = parked[SECTIONS - 1 - section_index]
        slot_rows = (jnp.arange(REPLICAS, dtype=jnp.int32)[:, None] * MB + slot_order[section_index]).reshape(-1).astype(jnp.int32)
        inputs = jnp.take(source, slot_rows, axis=0)
        inputs_wide = inputs.astype(jnp.float32)
        inverse = lax.rsqrt(lax.optimization_barrier(jnp.mean(inputs_wide * inputs_wide, axis=-1)) + EPSILON)
        scale_col = inverse[..., None]
        gain_full = norm_gain[section_index].astype(jnp.float32)
        normed = (inputs_wide * scale_col * gain_full).astype(jnp.bfloat16)
        weight = kv_weight[section_index]
        flat_normed = normed.reshape(BATCH * S, D)
        projected = jnp.dot(flat_normed, weight, preferred_element_type=jnp.float32).astype(jnp.bfloat16)
        projected = projected.reshape(BATCH, S, KVW)
        head_span = KVH * HD
        kv_grads = attention_grads(queries[section_index], out_grad[section_index], projected[..., :head_span], projected[..., head_span:], segment_ids[section_index])
        flat_grads = kv_grads.reshape(BATCH * S, KVW)
        weight_grad = lax.dot_general(flat_normed, flat_grads, (((0,), (0,)), ((), ())), preferred_element_type=jnp.float32).astype(jnp.bfloat16)
        normed_grad = lax.dot_general(flat_grads, weight, (((1,), (1,)), ((), ())), preferred_element_type=jnp.float32).reshape(BATCH, S, D)
        scaled_grad = normed_grad * gain_full
        inner_mean = lax.optimization_barrier(jnp.mean(scaled_grad * inputs_wide, axis=-1, keepdims=True))
        input_grad = (scale_col * scaled_grad - inputs_wide * scale_col ** 3 * inner_mean).astype(jnp.bfloat16)
        gain_grad = lax.optimization_barrier(jnp.sum(normed_grad * inputs_wide * scale_col, axis=(0, 1)))
        return (input_grad, weight_grad, gain_grad)
    input_grads, weight_grads, gain_grads = lax.map(one_section, jnp.arange(SECTIONS, dtype=jnp.int32))
    upstream_grad = jnp.concatenate([input_grads[1:], jnp.zeros_like(input_grads[:1])], axis=0)
    return (upstream_grad, weight_grads, gain_grads)
```

```python
import math

import jax
import jax.numpy as jnp
from jax import lax
from jax.sharding import PartitionSpec as P

QH = 32
KVH = 4
HD = 128


EPSILON = 1e-05


def attention_grads(queries, out_grad, keys, values, segments):
    batch_count = queries.shape[0]
    seq_len = queries.shape[1]
    group_size = QH // KVH
    scaling = 1.0 / math.sqrt(HD)
    query_heads = queries.reshape(batch_count, seq_len, KVH, group_size, HD)
    grad_heads = out_grad.reshape(batch_count, seq_len, KVH, group_size, HD)
    key_heads = keys.reshape(batch_count, seq_len, KVH, HD)
    value_heads = values.reshape(batch_count, seq_len, KVH, HD)
    scores = (
        jnp.einsum("bqhgd,bkhd->bhgqk", query_heads, key_heads, preferred_element_type=jnp.float32)
        * scaling
    )
    position = jnp.arange(seq_len)
    causal = position[None, :] <= position[:, None]
    allowed = causal[None] & (segments[:, :, None] == segments[:, None, :])
    scores = jnp.where(allowed[:, None, None], scores, -1e30)
    highest = jnp.max(scores, axis=-1, keepdims=True)
    weights = jnp.exp(scores - highest)
    probabilities = weights / jnp.sum(weights, axis=-1, keepdims=True)
    probs_low = probabilities.astype(jnp.bfloat16)
    value_grad = jnp.einsum(
        "bhgqk,bqhgd->bkhd", probs_low, grad_heads, preferred_element_type=jnp.float32
    )
    prob_grad = jnp.einsum(
        "bqhgd,bkhd->bhgqk", grad_heads, value_heads, preferred_element_type=jnp.float32
    )
    row_dot = jnp.sum(probabilities * prob_grad, axis=-1, keepdims=True)
    score_grad = (probabilities * (prob_grad - row_dot) * scaling).astype(jnp.bfloat16)
    key_grad = jnp.einsum(
        "bhgqk,bqhgd->bkhd", score_grad, query_heads, preferred_element_type=jnp.float32
    )
    key_low = key_grad.astype(jnp.bfloat16).reshape(batch_count, seq_len, KVH * HD)
    value_low = value_grad.astype(jnp.bfloat16).reshape(batch_count, seq_len, KVH * HD)
    return jnp.concatenate([key_low, value_low], axis=-1)


def local(parked, slot_order, segment_ids, queries, out_grad, norm_gain, kv_weight):
    sections = lax.axis_size("pipe")
    replicas = lax.axis_size("dp")
    me = lax.axis_index("dp")
    stored = parked[0]
    micro_count, seq_len, feature_count = stored.shape
    token_count = micro_count * seq_len
    width = feature_count // replicas
    axes = ("pipe", "dp")

    flat_stored = stored.reshape(token_count, feature_count)
    stored_wide = flat_stored.astype(jnp.float32)
    inv_src = lax.rsqrt(jnp.mean(stored_wide * stored_wide, axis=-1) + EPSILON)

    received = []
    for k in range(replicas):
        pairs = [
            (s * replicas + d, (sections - 1 - s) * replicas + (d + k) % replicas)
            for s in range(sections)
            for d in range(replicas)
        ]
        col = (me + k) % replicas
        block = lax.dynamic_slice_in_dim(flat_stored, col * width, width, axis=1)
        received.append(lax.ppermute((block, inv_src), axes, pairs))

    orders = lax.all_gather(slot_order[0, 0], "dp", axis=0, tiled=False)
    replica_ids = jnp.arange(replicas, dtype=jnp.int32)
    source_k = (me - replica_ids) % replicas
    rows = (source_k[:, None] * micro_count + orders).reshape(-1)
    blocks = jnp.stack([b for b, _ in received]).reshape(replicas * micro_count, seq_len, width)
    invs = jnp.stack([v for _, v in received]).reshape(replicas * micro_count, seq_len)
    x_cols = jnp.take(blocks, rows, axis=0).reshape(replicas * token_count, width)
    inverse = jnp.take(invs, rows, axis=0).reshape(replicas * token_count)

    gain_full = norm_gain[0].astype(jnp.float32)
    gain_local = lax.dynamic_slice_in_dim(gain_full, me * width, width)
    x_wide = x_cols.astype(jnp.float32)
    scale_col = inverse[:, None]
    normed = (x_wide * scale_col * gain_local).astype(jnp.bfloat16)
    local_weight = kv_weight[0]
    partial = jnp.dot(normed, local_weight, preferred_element_type=jnp.float32)
    projected = lax.psum_scatter(partial, "dp", scatter_dimension=0, tiled=True)
    projected_low = projected.astype(jnp.bfloat16).reshape(micro_count, seq_len, -1)
    head_span = projected_low.shape[-1] // 2
    kv_grads = attention_grads(
        queries[0],
        out_grad[0],
        projected_low[..., :head_span],
        projected_low[..., head_span:],
        segment_ids[0],
    )
    kv_grads = kv_grads.reshape(token_count, -1)
    all_kv_grads = lax.all_gather(kv_grads, "dp", axis=0, tiled=True)
    weight_grad = lax.dot_general(
        normed, all_kv_grads, (((0,), (0,)), ((), ())), preferred_element_type=jnp.float32
    ).astype(jnp.bfloat16)
    normed_grad = lax.dot_general(
        all_kv_grads, local_weight, (((1,), (1,)), ((), ())), preferred_element_type=jnp.float32
    )
    scaled_grad = normed_grad * gain_local
    inner_part = jnp.sum(scaled_grad * x_wide, axis=-1)
    inner_mean = jnp.sum(lax.all_gather(inner_part, "dp", axis=0), axis=0) / feature_count
    input_grad = (
        scale_col * scaled_grad - x_wide * scale_col**3 * inner_mean[:, None]
    ).astype(jnp.bfloat16)
    gain_part = jnp.sum(normed_grad * x_wide * scale_col, axis=0)
    gain_grad = lax.all_gather(gain_part, "dp", axis=0, tiled=True)

    upstream = jnp.zeros((token_count, feature_count), jnp.bfloat16)
    for k in range(replicas):
        pairs = [
            (s * replicas + d, (s - 1) * replicas + (d + k) % replicas)
            for s in range(1, sections)
            for d in range(replicas)
        ]
        dest = (me + k) % replicas
        block = lax.dynamic_slice_in_dim(input_grad, dest * token_count, token_count, axis=0)
        got = lax.ppermute(block, axes, pairs)
        upstream = lax.dynamic_update_slice_in_dim(
            upstream, got, ((me - k) % replicas) * width, axis=1
        )
    upstream = upstream.reshape(micro_count, seq_len, feature_count)
    return (upstream[None], weight_grad[None], gain_grad[None])


def solution(mesh):
    return jax.shard_map(
        local,
        mesh=mesh,
        in_specs=(
            P("pipe", "dp", None, None),
            P("pipe", "dp", None),
            P("pipe", "dp", None),
            P("pipe", "dp", None, None),
            P("pipe", "dp", None, None),
            P("pipe", None),
            P("pipe", "dp", None),
        ),
        out_specs=(P("pipe", "dp", None, None), P("pipe", "dp", None), P("pipe", None)),
        check_vma=False,
    )
```

```python
import math

import jax
import jax.numpy as jnp
from jax import lax
from jax.sharding import PartitionSpec as P


QH = 32
KVH = 4
HD = 128


EPSILON = 1e-05


def attention_grads(queries, out_grad, keys, values, segments):
    batch_count = queries.shape[0]
    seq_len = queries.shape[1]
    group_size = QH // KVH
    scaling = 1.0 / math.sqrt(HD)
    query_heads = queries.reshape(batch_count, seq_len, KVH, group_size, HD)
    grad_heads = out_grad.reshape(batch_count, seq_len, KVH, group_size, HD)
    key_heads = keys.reshape(batch_count, seq_len, KVH, HD)
    value_heads = values.reshape(batch_count, seq_len, KVH, HD)
    scores = (
        jnp.einsum("bqhgd,bkhd->bhgqk", query_heads, key_heads, preferred_element_type=jnp.float32)
        * scaling
    )
    position = jnp.arange(seq_len)
    causal = position[None, :] <= position[:, None]
    allowed = causal[None] & (segments[:, :, None] == segments[:, None, :])
    scores = jnp.where(allowed[:, None, None], scores, -1e30)
    highest = jnp.max(scores, axis=-1, keepdims=True)
    weights = jnp.exp(scores - highest)
    probabilities = weights / jnp.sum(weights, axis=-1, keepdims=True)
    probs_low = probabilities.astype(jnp.bfloat16)
    value_grad = jnp.einsum(
        "bhgqk,bqhgd->bkhd", probs_low, grad_heads, preferred_element_type=jnp.float32
    )
    prob_grad = jnp.einsum(
        "bqhgd,bkhd->bhgqk", grad_heads, value_heads, preferred_element_type=jnp.float32
    )
    row_dot = jnp.sum(probabilities * prob_grad, axis=-1, keepdims=True)
    score_grad = (probabilities * (prob_grad - row_dot) * scaling).astype(jnp.bfloat16)
    key_grad = jnp.einsum(
        "bhgqk,bqhgd->bkhd", score_grad, query_heads, preferred_element_type=jnp.float32
    )
    key_low = key_grad.astype(jnp.bfloat16).reshape(batch_count, seq_len, KVH * HD)
    value_low = value_grad.astype(jnp.bfloat16).reshape(batch_count, seq_len, KVH * HD)
    return jnp.concatenate([key_low, value_low], axis=-1)


def local(parked, slot_order, segment_ids, queries, out_grad, norm_gain, kv_weight):
    sections = lax.axis_size("pipe")
    replicas = lax.axis_size("dp")
    me = lax.axis_index("dp")
    stored = parked[0]
    micro_count, seq_len, feature_count = stored.shape
    width = feature_count // replicas
    axes = ("pipe", "dp")
    own_order = slot_order[0, 0]
    next_order = lax.ppermute(own_order, "pipe", [(s, s - 1) for s in range(1, sections)])

    gain_full = norm_gain[0].astype(jnp.float32)
    gain_local = lax.dynamic_slice_in_dim(gain_full, me * width, width)
    local_weight = kv_weight[0]
    replica_ids = jnp.arange(replicas, dtype=jnp.int32)
    source_k = (me - replica_ids) % replicas

    def send_slot(slot):
        tokens = stored[slot]
        tokens_wide = tokens.astype(jnp.float32)
        inv_src = lax.rsqrt(jnp.mean(tokens_wide * tokens_wide, axis=-1) + EPSILON)
        parts = []
        for k in range(replicas):
            col = (me + k) % replicas
            parts.append((lax.dynamic_slice_in_dim(tokens, col * width, width, axis=1), inv_src))
        return parts

    def move_slot(parts):
        received = []
        for k in range(replicas):
            pairs = [
                (s * replicas + d, (sections - 1 - s) * replicas + (d + k) % replicas)
                for s in range(sections)
                for d in range(replicas)
            ]
            received.append(lax.ppermute(parts[k], axes, pairs))
        return received

    received = [move_slot(send_slot(0))]
    later = send_slot(1)
    received[0], later = lax.optimization_barrier((received[0], later))
    received.append(move_slot(later))

    def work(slot, got):
        blocks = jnp.stack([b for b, _ in got])
        invs = jnp.stack([v for _, v in got])
        x_cols = jnp.take(blocks, source_k, axis=0).reshape(replicas * seq_len, width)
        inverse = jnp.take(invs, source_k, axis=0).reshape(replicas * seq_len)
        x_wide = x_cols.astype(jnp.float32)
        scale_col = inverse[:, None]
        normed = (x_wide * scale_col * gain_local).astype(jnp.bfloat16)
        partial = jnp.dot(normed, local_weight, preferred_element_type=jnp.float32)
        projected = lax.psum_scatter(partial, "dp", scatter_dimension=0, tiled=True)
        projected_low = projected.astype(jnp.bfloat16)[None]
        head_span = projected_low.shape[-1] // 2
        micro = jnp.argmax(own_order == slot).astype(jnp.int32)
        kv_grads = attention_grads(
            lax.dynamic_slice_in_dim(queries[0], micro, 1, axis=0),
            lax.dynamic_slice_in_dim(out_grad[0], micro, 1, axis=0),
            projected_low[..., :head_span],
            projected_low[..., head_span:],
            lax.dynamic_slice_in_dim(segment_ids[0], micro, 1, axis=0),
        )
        kv_grads = kv_grads.reshape(seq_len, -1)
        all_kv_grads = lax.all_gather(kv_grads, "dp", axis=0, tiled=True)
        weight_part = lax.dot_general(
            normed, all_kv_grads, (((0,), (0,)), ((), ())), preferred_element_type=jnp.float32
        )
        normed_grad = lax.dot_general(
            all_kv_grads, local_weight, (((1,), (1,)), ((), ())), preferred_element_type=jnp.float32
        )
        scaled_grad = normed_grad * gain_local
        inner_part = jnp.sum(scaled_grad * x_wide, axis=-1)
        inner_mean = jnp.sum(lax.all_gather(inner_part, "dp", axis=0), axis=0) / feature_count
        input_grad = (
            scale_col * scaled_grad - x_wide * scale_col**3 * inner_mean[:, None]
        ).astype(jnp.bfloat16)
        gain_part = jnp.sum(normed_grad * x_wide * scale_col, axis=0)
        return input_grad, weight_part, gain_part

    def send_back(input_grad):
        upstream = jnp.zeros((seq_len, feature_count), jnp.bfloat16)
        for k in range(replicas):
            pairs = [
                (s * replicas + d, (s - 1) * replicas + (d + k) % replicas)
                for s in range(1, sections)
                for d in range(replicas)
            ]
            dest = (me + k) % replicas
            block = lax.dynamic_slice_in_dim(input_grad, dest * seq_len, seq_len, axis=0)
            got_back = lax.ppermute(block, axes, pairs)
            upstream = lax.dynamic_update_slice_in_dim(
                upstream, got_back, ((me - k) % replicas) * width, axis=1
            )
        return upstream

    weight_acc = None
    gain_acc = None
    slot_grads = []
    for slot in range(micro_count):
        input_grad, weight_part, gain_part = work(slot, received[slot])
        if slot + 1 < micro_count:
            received[slot + 1], input_grad = lax.optimization_barrier(
                (received[slot + 1], input_grad)
            )
        weight_acc = weight_part if weight_acc is None else weight_acc + weight_part
        gain_acc = gain_part if gain_acc is None else gain_acc + gain_part
        slot_grads.append(send_back(input_grad))

    weight_grad = weight_acc.astype(jnp.bfloat16)
    gain_grad = lax.all_gather(gain_acc, "dp", axis=0, tiled=True)
    by_slot = jnp.stack(slot_grads)
    upstream = jnp.take(by_slot, next_order, axis=0)
    return (upstream[None], weight_grad[None], gain_grad[None])


def solution(mesh):
    return jax.shard_map(
        local,
        mesh=mesh,
        in_specs=(
            P("pipe", "dp", None, None),
            P("pipe", "dp", None),
            P("pipe", "dp", None),
            P("pipe", "dp", None, None),
            P("pipe", "dp", None, None),
            P("pipe", None),
            P("pipe", "dp", None),
        ),
        out_specs=(P("pipe", "dp", None, None), P("pipe", "dp", None), P("pipe", None)),
        check_vma=False,
    )
```

```python
import math

import jax
import jax.numpy as jnp
from jax import lax
from jax.sharding import PartitionSpec as P


QH = 32
KVH = 4
HD = 128


EPSILON = 1e-05


def attention_grads(queries, out_grad, keys, values, segments):
    batch_count = queries.shape[0]
    seq_len = queries.shape[1]
    group_size = QH // KVH
    scaling = 1.0 / math.sqrt(HD)
    query_heads = queries.reshape(batch_count, seq_len, KVH, group_size, HD)
    grad_heads = out_grad.reshape(batch_count, seq_len, KVH, group_size, HD)
    key_heads = keys.reshape(batch_count, seq_len, KVH, HD)
    value_heads = values.reshape(batch_count, seq_len, KVH, HD)
    scores = (
        jnp.einsum("bqhgd,bkhd->bhgqk", query_heads, key_heads, preferred_element_type=jnp.float32)
        * scaling
    )
    position = jnp.arange(seq_len)
    causal = position[None, :] <= position[:, None]
    allowed = causal[None] & (segments[:, :, None] == segments[:, None, :])
    scores = jnp.where(allowed[:, None, None], scores, -1e30)
    highest = jnp.max(scores, axis=-1, keepdims=True)
    weights = jnp.exp(scores - highest)
    probabilities = weights / jnp.sum(weights, axis=-1, keepdims=True)
    probs_low = probabilities.astype(jnp.bfloat16)
    value_grad = jnp.einsum(
        "bhgqk,bqhgd->bkhd", probs_low, grad_heads, preferred_element_type=jnp.float32
    )
    prob_grad = jnp.einsum(
        "bqhgd,bkhd->bhgqk", grad_heads, value_heads, preferred_element_type=jnp.float32
    )
    row_dot = jnp.sum(probabilities * prob_grad, axis=-1, keepdims=True)
    score_grad = (probabilities * (prob_grad - row_dot) * scaling).astype(jnp.bfloat16)
    key_grad = jnp.einsum(
        "bhgqk,bqhgd->bkhd", score_grad, query_heads, preferred_element_type=jnp.float32
    )
    key_low = key_grad.astype(jnp.bfloat16).reshape(batch_count, seq_len, KVH * HD)
    value_low = value_grad.astype(jnp.bfloat16).reshape(batch_count, seq_len, KVH * HD)
    return jnp.concatenate([key_low, value_low], axis=-1)


def local(parked, slot_order, segment_ids, queries, out_grad, norm_gain, kv_weight):
    sections = lax.axis_size("pipe")
    replicas = lax.axis_size("dp")
    me = lax.axis_index("dp")
    stored = parked[0]
    micro_count, seq_len, feature_count = stored.shape
    width = feature_count // replicas
    axes = ("pipe", "dp")
    own_order = slot_order[0, 0]
    next_order = lax.ppermute(own_order, "pipe", [(s, s - 1) for s in range(1, sections)])

    gain_full = norm_gain[0].astype(jnp.float32)
    gain_local = lax.dynamic_slice_in_dim(gain_full, me * width, width)
    local_weight = kv_weight[0]
    replica_ids = jnp.arange(replicas, dtype=jnp.int32)
    source_k = (me - replica_ids) % replicas

    def send_slot(slot):
        tokens = stored[slot]
        parts = []
        for k in range(replicas):
            col = (me + k) % replicas
            parts.append(lax.dynamic_slice_in_dim(tokens, col * width, width, axis=1))
        return parts

    def move_slot(parts):
        received = []
        for k in range(replicas):
            pairs = [
                (s * replicas + d, (sections - 1 - s) * replicas + (d + k) % replicas)
                for s in range(sections)
                for d in range(replicas)
            ]
            received.append(lax.ppermute(parts[k], axes, pairs))
        return received

    received = [move_slot(send_slot(0))]
    later = send_slot(1)
    received[0], later = lax.optimization_barrier((received[0], later))
    received.append(move_slot(later))

    def work(slot, got):
        blocks = jnp.stack(got)
        x_cols = jnp.take(blocks, source_k, axis=0).reshape(replicas * seq_len, width)
        x_wide = x_cols.astype(jnp.float32)
        square_part = jnp.sum(x_wide * x_wide, axis=-1)
        square_sum = jnp.sum(lax.all_gather(square_part, "dp", axis=0), axis=0)
        inverse = lax.rsqrt(square_sum / feature_count + EPSILON)
        scale_col = inverse[:, None]
        normed = (x_wide * scale_col * gain_local).astype(jnp.bfloat16)
        partial = jnp.dot(normed, local_weight, preferred_element_type=jnp.float32)
        projected = lax.psum_scatter(partial, "dp", scatter_dimension=0, tiled=True)
        projected_low = projected.astype(jnp.bfloat16)[None]
        head_span = projected_low.shape[-1] // 2
        micro = jnp.argmax(own_order == slot).astype(jnp.int32)
        kv_grads = attention_grads(
            lax.dynamic_slice_in_dim(queries[0], micro, 1, axis=0),
            lax.dynamic_slice_in_dim(out_grad[0], micro, 1, axis=0),
            projected_low[..., :head_span],
            projected_low[..., head_span:],
            lax.dynamic_slice_in_dim(segment_ids[0], micro, 1, axis=0),
        )
        kv_grads = kv_grads.reshape(seq_len, -1)
        all_kv_grads = lax.all_gather(kv_grads, "dp", axis=0, tiled=True)
        weight_part = lax.dot_general(
            normed, all_kv_grads, (((0,), (0,)), ((), ())), preferred_element_type=jnp.float32
        )
        normed_grad = lax.dot_general(
            all_kv_grads, local_weight, (((1,), (1,)), ((), ())), preferred_element_type=jnp.float32
        )
        scaled_grad = normed_grad * gain_local
        inner_part = jnp.sum(scaled_grad * x_wide, axis=-1)
        inner_mean = jnp.sum(lax.all_gather(inner_part, "dp", axis=0), axis=0) / feature_count
        input_grad = (
            scale_col * scaled_grad - x_wide * scale_col**3 * inner_mean[:, None]
        ).astype(jnp.bfloat16)
        gain_part = jnp.sum(normed_grad * x_wide * scale_col, axis=0)
        return input_grad, weight_part, gain_part

    def send_back(input_grad):
        upstream = jnp.zeros((seq_len, feature_count), jnp.bfloat16)
        for k in range(replicas):
            pairs = [
                (s * replicas + d, (s - 1) * replicas + (d + k) % replicas)
                for s in range(1, sections)
                for d in range(replicas)
            ]
            dest = (me + k) % replicas
            block = lax.dynamic_slice_in_dim(input_grad, dest * seq_len, seq_len, axis=0)
            got_back = lax.ppermute(block, axes, pairs)
            upstream = lax.dynamic_update_slice_in_dim(
                upstream, got_back, ((me - k) % replicas) * width, axis=1
            )
        return upstream

    weight_acc = None
    gain_acc = None
    slot_grads = []
    for slot in range(micro_count):
        input_grad, weight_part, gain_part = work(slot, received[slot])
        if slot + 1 < micro_count:
            received[slot + 1], input_grad = lax.optimization_barrier(
                (received[slot + 1], input_grad)
            )
        weight_acc = weight_part if weight_acc is None else weight_acc + weight_part
        gain_acc = gain_part if gain_acc is None else gain_acc + gain_part
        slot_grads.append(send_back(input_grad))

    weight_grad = weight_acc.astype(jnp.bfloat16)
    gain_grad = lax.all_gather(gain_acc, "dp", axis=0, tiled=True)
    by_slot = jnp.stack(slot_grads)
    upstream = jnp.take(by_slot, next_order, axis=0)
    return (upstream[None], weight_grad[None], gain_grad[None])


def solution(mesh):
    return jax.shard_map(
        local,
        mesh=mesh,
        in_specs=(
            P("pipe", "dp", None, None),
            P("pipe", "dp", None),
            P("pipe", "dp", None),
            P("pipe", "dp", None, None),
            P("pipe", "dp", None, None),
            P("pipe", None),
            P("pipe", "dp", None),
        ),
        out_specs=(P("pipe", "dp", None, None), P("pipe", "dp", None), P("pipe", None)),
        check_vma=False,
    )
```

```python
import math

import jax
import jax.numpy as jnp
from jax import lax
from jax.sharding import PartitionSpec as P


QH = 32
KVH = 4
HD = 128


EPSILON = 1e-05


def attention_grads(queries, out_grad, keys, values, segments):
    batch_count = queries.shape[0]
    seq_len = queries.shape[1]
    group_size = QH // KVH
    scaling = 1.0 / math.sqrt(HD)
    query_heads = queries.reshape(batch_count, seq_len, KVH, group_size, HD)
    grad_heads = out_grad.reshape(batch_count, seq_len, KVH, group_size, HD)
    key_heads = keys.reshape(batch_count, seq_len, KVH, HD)
    value_heads = values.reshape(batch_count, seq_len, KVH, HD)
    scores = (
        jnp.einsum("bqhgd,bkhd->bhgqk", query_heads, key_heads, preferred_element_type=jnp.float32)
        * scaling
    )
    position = jnp.arange(seq_len)
    causal = position[None, :] <= position[:, None]
    allowed = causal[None] & (segments[:, :, None] == segments[:, None, :])
    scores = jnp.where(allowed[:, None, None], scores, -1e30)
    highest = jnp.max(scores, axis=-1, keepdims=True)
    weights = jnp.exp(scores - highest)
    probabilities = weights / jnp.sum(weights, axis=-1, keepdims=True)
    probs_low = probabilities.astype(jnp.bfloat16)
    value_grad = jnp.einsum(
        "bhgqk,bqhgd->bkhd", probs_low, grad_heads, preferred_element_type=jnp.float32
    )
    prob_grad = jnp.einsum(
        "bqhgd,bkhd->bhgqk", grad_heads, value_heads, preferred_element_type=jnp.float32
    )
    row_dot = jnp.sum(probabilities * prob_grad, axis=-1, keepdims=True)
    score_grad = (probabilities * (prob_grad - row_dot) * scaling).astype(jnp.bfloat16)
    key_grad = jnp.einsum(
        "bhgqk,bqhgd->bkhd", score_grad, query_heads, preferred_element_type=jnp.float32
    )
    key_low = key_grad.astype(jnp.bfloat16).reshape(batch_count, seq_len, KVH * HD)
    value_low = value_grad.astype(jnp.bfloat16).reshape(batch_count, seq_len, KVH * HD)
    return jnp.concatenate([key_low, value_low], axis=-1)


def local(parked, slot_order, segment_ids, queries, out_grad, norm_gain, kv_weight):
    sections = lax.axis_size("pipe")
    replicas = lax.axis_size("dp")
    me = lax.axis_index("dp")
    stored = parked[0]
    _, seq_len, feature_count = stored.shape
    width = feature_count // replicas
    axes = ("pipe", "dp")
    own_order = slot_order[0, 0]
    next_order = lax.ppermute(own_order, "pipe", [(s, s - 1) for s in range(1, sections)])

    gain_full = norm_gain[0].astype(jnp.float32)
    gain_local = lax.dynamic_slice_in_dim(gain_full, me * width, width)
    local_weight = kv_weight[0]
    replica_ids = jnp.arange(replicas, dtype=jnp.int32)
    source_k = (me - replica_ids) % replicas

    def send_slot(slot):
        tokens = stored[slot]
        parts = []
        for k in range(replicas):
            col = (me + k) % replicas
            parts.append(lax.dynamic_slice_in_dim(tokens, col * width, width, axis=1))
        return parts

    def move_slot(parts):
        received = []
        for k in range(replicas):
            pairs = [
                (s * replicas + d, (sections - 1 - s) * replicas + (d + k) % replicas)
                for s in range(sections)
                for d in range(replicas)
            ]
            received.append(lax.ppermute(parts[k], axes, pairs))
        return received

    received = [move_slot(send_slot(0))]
    later = send_slot(1)
    received[0], later = lax.optimization_barrier((received[0], later))
    received.append(move_slot(later))

    def work_front(got):
        blocks = jnp.stack(got)
        x_cols = jnp.take(blocks, source_k, axis=0).reshape(replicas * seq_len, width)
        x_wide = x_cols.astype(jnp.float32)
        square_part = jnp.sum(x_wide * x_wide, axis=-1)
        square_sum = jnp.sum(lax.all_gather(square_part, "dp", axis=0), axis=0)
        inverse = lax.rsqrt(square_sum / feature_count + EPSILON)
        scale_col = inverse[:, None]
        normed = (x_wide * scale_col * gain_local).astype(jnp.bfloat16)
        partial = jnp.dot(normed, local_weight, preferred_element_type=jnp.float32)
        return partial, (x_wide, scale_col, normed)

    def work_mid(slot, partial):
        projected = lax.psum_scatter(partial, "dp", scatter_dimension=0, tiled=True)
        projected_low = projected.astype(jnp.bfloat16)[None]
        head_span = projected_low.shape[-1] // 2
        micro = jnp.argmax(own_order == slot).astype(jnp.int32)
        kv_grads = attention_grads(
            lax.dynamic_slice_in_dim(queries[0], micro, 1, axis=0),
            lax.dynamic_slice_in_dim(out_grad[0], micro, 1, axis=0),
            projected_low[..., :head_span],
            projected_low[..., head_span:],
            lax.dynamic_slice_in_dim(segment_ids[0], micro, 1, axis=0),
        )
        kv_grads = kv_grads.reshape(seq_len, -1)
        return kv_grads

    def work_back(all_kv_grads, kept):
        x_wide, scale_col, normed = kept
        weight_part = lax.dot_general(
            normed, all_kv_grads, (((0,), (0,)), ((), ())), preferred_element_type=jnp.float32
        )
        normed_grad = lax.dot_general(
            all_kv_grads, local_weight, (((1,), (1,)), ((), ())), preferred_element_type=jnp.float32
        )
        scaled_grad = normed_grad * gain_local
        inner_part = jnp.sum(scaled_grad * x_wide, axis=-1)
        inner_mean = jnp.sum(lax.all_gather(inner_part, "dp", axis=0), axis=0) / feature_count
        input_grad = (
            scale_col * scaled_grad - x_wide * scale_col**3 * inner_mean[:, None]
        ).astype(jnp.bfloat16)
        gain_part = jnp.sum(normed_grad * x_wide * scale_col, axis=0)
        return input_grad, weight_part, gain_part

    def send_back(input_grad):
        upstream = jnp.zeros((seq_len, feature_count), jnp.bfloat16)
        for k in range(replicas):
            pairs = [
                (s * replicas + d, (s - 1) * replicas + (d + k) % replicas)
                for s in range(1, sections)
                for d in range(replicas)
            ]
            dest = (me + k) % replicas
            block = lax.dynamic_slice_in_dim(input_grad, dest * seq_len, seq_len, axis=0)
            got_back = lax.ppermute(block, axes, pairs)
            upstream = lax.dynamic_update_slice_in_dim(
                upstream, got_back, ((me - k) % replicas) * width, axis=1
            )
        return upstream

    partial0, kept0 = work_front(received[0])
    kv0 = work_mid(0, partial0)
    received[1], (kv0, kept0) = lax.optimization_barrier((received[1], (kv0, kept0)))
    partial1, kept1 = work_front(received[1])
    all_kv0 = lax.all_gather(kv0, "dp", axis=0, tiled=True)
    all_kv0, partial1 = lax.optimization_barrier((all_kv0, partial1))
    kv1 = work_mid(1, partial1)
    grad0, weight_acc, gain_acc = work_back(all_kv0, kept0)
    kv1, grad0 = lax.optimization_barrier((kv1, grad0))
    all_kv1 = lax.all_gather(kv1, "dp", axis=0, tiled=True)
    grad1, weight_part, gain_part = work_back(all_kv1, kept1)
    weight_acc = weight_acc + weight_part
    gain_acc = gain_acc + gain_part
    slot_grads = [send_back(grad0), send_back(grad1)]

    weight_grad = weight_acc.astype(jnp.bfloat16)
    gain_grad = lax.all_gather(gain_acc, "dp", axis=0, tiled=True)
    by_slot = jnp.stack(slot_grads)
    upstream = jnp.take(by_slot, next_order, axis=0)
    return (upstream[None], weight_grad[None], gain_grad[None])


def solution(mesh):
    return jax.shard_map(
        local,
        mesh=mesh,
        in_specs=(
            P("pipe", "dp", None, None),
            P("pipe", "dp", None),
            P("pipe", "dp", None),
            P("pipe", "dp", None, None),
            P("pipe", "dp", None, None),
            P("pipe", None),
            P("pipe", "dp", None),
        ),
        out_specs=(P("pipe", "dp", None, None), P("pipe", "dp", None), P("pipe", None)),
        check_vma=False,
    )
```

```python
import math

import jax
import jax.numpy as jnp
from jax import lax
from jax.sharding import PartitionSpec as P


QH = 32
KVH = 4
HD = 128


EPSILON = 1e-05


def attention_grads(queries, out_grad, keys, values, segments):
    batch_count = queries.shape[0]
    seq_len = queries.shape[1]
    group_size = QH // KVH
    scaling = 1.0 / math.sqrt(HD)
    query_heads = queries.reshape(batch_count, seq_len, KVH, group_size, HD)
    grad_heads = out_grad.reshape(batch_count, seq_len, KVH, group_size, HD)
    key_heads = keys.reshape(batch_count, seq_len, KVH, HD)
    value_heads = values.reshape(batch_count, seq_len, KVH, HD)
    scores = (
        jnp.einsum("bqhgd,bkhd->bhgqk", query_heads, key_heads, preferred_element_type=jnp.float32)
        * scaling
    )
    position = jnp.arange(seq_len)
    causal = position[None, :] <= position[:, None]
    allowed = causal[None] & (segments[:, :, None] == segments[:, None, :])
    scores = jnp.where(allowed[:, None, None], scores, -1e30)
    highest = jnp.max(scores, axis=-1, keepdims=True)
    weights = jnp.exp(scores - highest)
    probabilities = weights / jnp.sum(weights, axis=-1, keepdims=True)
    probs_low = probabilities.astype(jnp.bfloat16)
    value_grad = jnp.einsum(
        "bhgqk,bqhgd->bkhd", probs_low, grad_heads, preferred_element_type=jnp.float32
    )
    prob_grad = jnp.einsum(
        "bqhgd,bkhd->bhgqk", grad_heads, value_heads, preferred_element_type=jnp.float32
    )
    row_dot = jnp.sum(probabilities * prob_grad, axis=-1, keepdims=True)
    score_grad = (probabilities * (prob_grad - row_dot) * scaling).astype(jnp.bfloat16)
    key_grad = jnp.einsum(
        "bhgqk,bqhgd->bkhd", score_grad, query_heads, preferred_element_type=jnp.float32
    )
    key_low = key_grad.astype(jnp.bfloat16).reshape(batch_count, seq_len, KVH * HD)
    value_low = value_grad.astype(jnp.bfloat16).reshape(batch_count, seq_len, KVH * HD)
    return jnp.concatenate([key_low, value_low], axis=-1)


def dp_reduce_scatter(partial, replicas, me):
    rows = partial.shape[0] // replicas
    total = lax.dynamic_slice_in_dim(partial, me * rows, rows, axis=0)
    for k in range(1, replicas):
        dest = (me + k) % replicas
        block = lax.dynamic_slice_in_dim(partial, dest * rows, rows, axis=0)
        total = total + lax.ppermute(
            block, "dp", [(d, (d + k) % replicas) for d in range(replicas)]
        )
    return total


def dp_all_gather(block, replicas, me):
    parts = [block]
    for k in range(1, replicas):
        parts.append(lax.ppermute(block, "dp", [(d, (d + k) % replicas) for d in range(replicas)]))
    order = (me - jnp.arange(replicas, dtype=jnp.int32)) % replicas
    gathered = jnp.take(jnp.stack(parts), order, axis=0)
    return gathered.reshape(replicas * block.shape[0], *block.shape[1:])


def local(parked, slot_order, segment_ids, queries, out_grad, norm_gain, kv_weight):
    sections = lax.axis_size("pipe")
    replicas = lax.axis_size("dp")
    me = lax.axis_index("dp")
    stored = parked[0]
    _, seq_len, feature_count = stored.shape
    width = feature_count // replicas
    axes = ("pipe", "dp")
    own_order = slot_order[0, 0]
    next_order = lax.ppermute(own_order, "pipe", [(s, s - 1) for s in range(1, sections)])

    gain_full = norm_gain[0].astype(jnp.float32)
    gain_local = lax.dynamic_slice_in_dim(gain_full, me * width, width)
    local_weight = kv_weight[0]
    replica_ids = jnp.arange(replicas, dtype=jnp.int32)
    source_k = (me - replica_ids) % replicas

    def send_slot(slot):
        tokens = stored[slot]
        parts = []
        for k in range(replicas):
            col = (me + k) % replicas
            parts.append(lax.dynamic_slice_in_dim(tokens, col * width, width, axis=1))
        return parts

    def move_slot(parts):
        received = []
        for k in range(replicas):
            pairs = [
                (s * replicas + d, (sections - 1 - s) * replicas + (d + k) % replicas)
                for s in range(sections)
                for d in range(replicas)
            ]
            received.append(lax.ppermute(parts[k], axes, pairs))
        return received

    received = [move_slot(send_slot(0))]
    later = send_slot(1)
    received[0], later = lax.optimization_barrier((received[0], later))
    received.append(move_slot(later))

    def work_front(got):
        blocks = jnp.stack(got)
        x_cols = jnp.take(blocks, source_k, axis=0).reshape(replicas * seq_len, width)
        x_wide = x_cols.astype(jnp.float32)
        square_part = jnp.sum(x_wide * x_wide, axis=-1)
        square_sum = jnp.sum(lax.all_gather(square_part, "dp", axis=0), axis=0)
        inverse = lax.rsqrt(square_sum / feature_count + EPSILON)
        scale_col = inverse[:, None]
        normed = (x_wide * scale_col * gain_local).astype(jnp.bfloat16)
        partial = jnp.dot(normed, local_weight, preferred_element_type=jnp.float32)
        return partial, (x_wide, scale_col, normed)

    def work_mid(slot, partial):
        projected = dp_reduce_scatter(partial, replicas, me)
        projected_low = projected.astype(jnp.bfloat16)[None]
        head_span = projected_low.shape[-1] // 2
        micro = jnp.argmax(own_order == slot).astype(jnp.int32)
        kv_grads = attention_grads(
            lax.dynamic_slice_in_dim(queries[0], micro, 1, axis=0),
            lax.dynamic_slice_in_dim(out_grad[0], micro, 1, axis=0),
            projected_low[..., :head_span],
            projected_low[..., head_span:],
            lax.dynamic_slice_in_dim(segment_ids[0], micro, 1, axis=0),
        )
        kv_grads = kv_grads.reshape(seq_len, -1)
        return kv_grads

    def work_back(all_kv_grads, kept):
        x_wide, scale_col, normed = kept
        weight_part = lax.dot_general(
            normed, all_kv_grads, (((0,), (0,)), ((), ())), preferred_element_type=jnp.float32
        )
        normed_grad = lax.dot_general(
            all_kv_grads, local_weight, (((1,), (1,)), ((), ())), preferred_element_type=jnp.float32
        )
        scaled_grad = normed_grad * gain_local
        inner_part = jnp.sum(scaled_grad * x_wide, axis=-1)
        inner_mean = jnp.sum(lax.all_gather(inner_part, "dp", axis=0), axis=0) / feature_count
        input_grad = (
            scale_col * scaled_grad - x_wide * scale_col**3 * inner_mean[:, None]
        ).astype(jnp.bfloat16)
        gain_part = jnp.sum(normed_grad * x_wide * scale_col, axis=0)
        return input_grad, weight_part, gain_part

    def send_back(input_grad):
        upstream = jnp.zeros((seq_len, feature_count), jnp.bfloat16)
        for k in range(replicas):
            pairs = [
                (s * replicas + d, (s - 1) * replicas + (d + k) % replicas)
                for s in range(1, sections)
                for d in range(replicas)
            ]
            dest = (me + k) % replicas
            block = lax.dynamic_slice_in_dim(input_grad, dest * seq_len, seq_len, axis=0)
            got_back = lax.ppermute(block, axes, pairs)
            upstream = lax.dynamic_update_slice_in_dim(
                upstream, got_back, ((me - k) % replicas) * width, axis=1
            )
        return upstream

    partial0, kept0 = work_front(received[0])
    kv0 = work_mid(0, partial0)
    received[1], (kv0, kept0) = lax.optimization_barrier((received[1], (kv0, kept0)))
    partial1, kept1 = work_front(received[1])
    all_kv0 = dp_all_gather(kv0, replicas, me)
    all_kv0, partial1 = lax.optimization_barrier((all_kv0, partial1))
    kv1 = work_mid(1, partial1)
    grad0, weight_acc, gain_acc = work_back(all_kv0, kept0)
    kv1, grad0 = lax.optimization_barrier((kv1, grad0))
    all_kv1 = dp_all_gather(kv1, replicas, me)
    grad1, weight_part, gain_part = work_back(all_kv1, kept1)
    weight_acc = weight_acc + weight_part
    gain_acc = gain_acc + gain_part
    slot_grads = [send_back(grad0), send_back(grad1)]

    weight_grad = weight_acc.astype(jnp.bfloat16)
    gain_grad = lax.all_gather(gain_acc, "dp", axis=0, tiled=True)
    by_slot = jnp.stack(slot_grads)
    upstream = jnp.take(by_slot, next_order, axis=0)
    return (upstream[None], weight_grad[None], gain_grad[None])


def solution(mesh):
    return jax.shard_map(
        local,
        mesh=mesh,
        in_specs=(
            P("pipe", "dp", None, None),
            P("pipe", "dp", None),
            P("pipe", "dp", None),
            P("pipe", "dp", None, None),
            P("pipe", "dp", None, None),
            P("pipe", None),
            P("pipe", "dp", None),
        ),
        out_specs=(P("pipe", "dp", None, None), P("pipe", "dp", None), P("pipe", None)),
        check_vma=False,
    )
```

```python
import math

import jax
import jax.numpy as jnp
from jax import lax
from jax.sharding import PartitionSpec as P


QH = 32
KVH = 4
HD = 128


EPSILON = 1e-05


def attention_grads(queries, out_grad, keys, values, segments):
    batch_count = queries.shape[0]
    seq_len = queries.shape[1]
    group_size = QH // KVH
    scaling = 1.0 / math.sqrt(HD)
    query_heads = queries.reshape(batch_count, seq_len, KVH, group_size, HD)
    grad_heads = out_grad.reshape(batch_count, seq_len, KVH, group_size, HD)
    key_heads = keys.reshape(batch_count, seq_len, KVH, HD)
    value_heads = values.reshape(batch_count, seq_len, KVH, HD)
    scores = (
        jnp.einsum("bqhgd,bkhd->bhgqk", query_heads, key_heads, preferred_element_type=jnp.float32)
        * scaling
    )
    position = jnp.arange(seq_len)
    causal = position[None, :] <= position[:, None]
    allowed = causal[None] & (segments[:, :, None] == segments[:, None, :])
    scores = jnp.where(allowed[:, None, None], scores, -1e30)
    highest = jnp.max(scores, axis=-1, keepdims=True)
    weights = jnp.exp(scores - highest)
    probabilities = weights / jnp.sum(weights, axis=-1, keepdims=True)
    probs_low = probabilities.astype(jnp.bfloat16)
    value_grad = jnp.einsum(
        "bhgqk,bqhgd->bkhd", probs_low, grad_heads, preferred_element_type=jnp.float32
    )
    prob_grad = jnp.einsum(
        "bqhgd,bkhd->bhgqk", grad_heads, value_heads, preferred_element_type=jnp.float32
    )
    row_dot = jnp.sum(probabilities * prob_grad, axis=-1, keepdims=True)
    score_grad = (probabilities * (prob_grad - row_dot) * scaling).astype(jnp.bfloat16)
    key_grad = jnp.einsum(
        "bhgqk,bqhgd->bkhd", score_grad, query_heads, preferred_element_type=jnp.float32
    )
    key_low = key_grad.astype(jnp.bfloat16).reshape(batch_count, seq_len, KVH * HD)
    value_low = value_grad.astype(jnp.bfloat16).reshape(batch_count, seq_len, KVH * HD)
    return jnp.concatenate([key_low, value_low], axis=-1)


def dp_reduce_scatter(partial, replicas, me):
    rows = partial.shape[0] // replicas
    total = lax.dynamic_slice_in_dim(partial, me * rows, rows, axis=0)
    for k in range(1, replicas):
        dest = (me + k) % replicas
        block = lax.dynamic_slice_in_dim(partial, dest * rows, rows, axis=0)
        total = total + lax.ppermute(
            block, "dp", [(d, (d + k) % replicas) for d in range(replicas)]
        )
    return total


def dp_all_gather(block, replicas, me):
    parts = [block]
    for k in range(1, replicas):
        parts.append(lax.ppermute(block, "dp", [(d, (d + k) % replicas) for d in range(replicas)]))
    order = (me - jnp.arange(replicas, dtype=jnp.int32)) % replicas
    gathered = jnp.take(jnp.stack(parts), order, axis=0)
    return gathered.reshape(replicas * block.shape[0], *block.shape[1:])


def local(parked, slot_order, segment_ids, queries, out_grad, norm_gain, kv_weight):
    sections = lax.axis_size("pipe")
    replicas = lax.axis_size("dp")
    me = lax.axis_index("dp")
    stored = parked[0]
    micro_count, seq_len, feature_count = stored.shape
    width = feature_count // replicas
    axes = ("pipe", "dp")
    own_order = slot_order[0, 0]
    next_order = lax.ppermute(own_order, "pipe", [(s, s - 1) for s in range(1, sections)])

    gain_full = norm_gain[0].astype(jnp.float32)
    gain_local = lax.dynamic_slice_in_dim(gain_full, me * width, width)
    local_weight = kv_weight[0]
    replica_ids = jnp.arange(replicas, dtype=jnp.int32)
    source_k = (me - replica_ids) % replicas

    def send_slot(slot):
        tokens = stored[slot]
        parts = []
        for k in range(replicas):
            col = (me + k) % replicas
            parts.append(lax.dynamic_slice_in_dim(tokens, col * width, width, axis=1))
        return parts

    def move_slot(parts):
        received = []
        for k in range(replicas):
            pairs = [
                (s * replicas + d, (sections - 1 - s) * replicas + (d + k) % replicas)
                for s in range(sections)
                for d in range(replicas)
            ]
            received.append(lax.ppermute(parts[k], axes, pairs))
        return received

    received = [move_slot(send_slot(0))]
    later = send_slot(1)
    received[0], later = lax.optimization_barrier((received[0], later))
    received.append(move_slot(later))

    def work_front(got):
        blocks = jnp.stack(got)
        x_cols = jnp.take(blocks, source_k, axis=0).reshape(replicas * seq_len, width)
        x_wide = x_cols.astype(jnp.float32)
        square_part = jnp.sum(x_wide * x_wide, axis=-1)
        square_sum = jnp.sum(dp_all_gather(square_part, replicas, me).reshape(replicas, -1), axis=0)
        inverse = lax.rsqrt(square_sum / feature_count + EPSILON)
        scale_col = inverse[:, None]
        normed = (x_wide * scale_col * gain_local).astype(jnp.bfloat16)
        partial = jnp.dot(normed, local_weight, preferred_element_type=jnp.float32)
        return partial, (x_wide, scale_col, normed)

    def work_mid(slot, partial):
        projected = dp_reduce_scatter(partial, replicas, me)
        projected_low = projected.astype(jnp.bfloat16)[None]
        head_span = projected_low.shape[-1] // 2
        micro = jnp.argmax(own_order == slot).astype(jnp.int32)
        kv_grads = attention_grads(
            lax.dynamic_slice_in_dim(queries[0], micro, 1, axis=0),
            lax.dynamic_slice_in_dim(out_grad[0], micro, 1, axis=0),
            projected_low[..., :head_span],
            projected_low[..., head_span:],
            lax.dynamic_slice_in_dim(segment_ids[0], micro, 1, axis=0),
        )
        kv_grads = kv_grads.reshape(seq_len, -1)
        return kv_grads

    def work_back(all_kv_grads, kept):
        x_wide, scale_col, normed = kept
        weight_part = lax.dot_general(
            normed, all_kv_grads, (((0,), (0,)), ((), ())), preferred_element_type=jnp.float32
        )
        normed_grad = lax.dot_general(
            all_kv_grads, local_weight, (((1,), (1,)), ((), ())), preferred_element_type=jnp.float32
        )
        scaled_grad = normed_grad * gain_local
        inner_part = jnp.sum(scaled_grad * x_wide, axis=-1)
        inner_sum = jnp.sum(dp_all_gather(inner_part, replicas, me).reshape(replicas, -1), axis=0)
        inner_mean = inner_sum / feature_count
        input_grad = (
            scale_col * scaled_grad - x_wide * scale_col**3 * inner_mean[:, None]
        ).astype(jnp.bfloat16)
        gain_part = jnp.sum(normed_grad * x_wide * scale_col, axis=0)
        return input_grad, weight_part, gain_part

    def send_back(slot, input_grad, upstream):
        micro = jnp.argmax(next_order == slot).astype(jnp.int32)
        for k in range(replicas):
            pairs = [
                (s * replicas + d, (s - 1) * replicas + (d + k) % replicas)
                for s in range(1, sections)
                for d in range(replicas)
            ]
            dest = (me + k) % replicas
            block = lax.dynamic_slice_in_dim(input_grad, dest * seq_len, seq_len, axis=0)
            got_back = lax.ppermute(block, axes, pairs)
            upstream = lax.dynamic_update_slice(
                upstream, got_back[None], (micro, 0, ((me - k) % replicas) * width)
            )
        return upstream

    partial0, kept0 = work_front(received[0])
    kv0 = work_mid(0, partial0)
    received[1], (kv0, kept0) = lax.optimization_barrier((received[1], (kv0, kept0)))
    partial1, kept1 = work_front(received[1])
    all_kv0 = dp_all_gather(kv0, replicas, me)
    all_kv0, partial1 = lax.optimization_barrier((all_kv0, partial1))
    kv1 = work_mid(1, partial1)
    grad0, weight_acc, gain_acc = work_back(all_kv0, kept0)
    kv1, grad0 = lax.optimization_barrier((kv1, grad0))
    all_kv1 = dp_all_gather(kv1, replicas, me)
    grad1, weight_part, gain_part = work_back(all_kv1, kept1)
    weight_acc = weight_acc + weight_part
    gain_acc = gain_acc + gain_part
    upstream = jnp.zeros((micro_count, seq_len, feature_count), jnp.bfloat16)
    upstream = send_back(0, grad0, upstream)
    upstream = send_back(1, grad1, upstream)

    weight_grad = weight_acc.astype(jnp.bfloat16)
    gain_grad = lax.all_gather(gain_acc, "dp", axis=0, tiled=True)
    return (upstream[None], weight_grad[None], gain_grad[None])


def solution(mesh):
    return jax.shard_map(
        local,
        mesh=mesh,
        in_specs=(
            P("pipe", "dp", None, None),
            P("pipe", "dp", None),
            P("pipe", "dp", None),
            P("pipe", "dp", None, None),
            P("pipe", "dp", None, None),
            P("pipe", None),
            P("pipe", "dp", None),
        ),
        out_specs=(P("pipe", "dp", None, None), P("pipe", "dp", None), P("pipe", None)),
        check_vma=False,
    )
```

```python
import math

import jax
import jax.numpy as jnp
from jax import lax
from jax.sharding import PartitionSpec as P


QH = 32
KVH = 4
HD = 128


EPSILON = 1e-05


def attention_grads(queries, out_grad, keys, values, segments):
    batch_count = queries.shape[0]
    seq_len = queries.shape[1]
    group_size = QH // KVH
    scaling = 1.0 / math.sqrt(HD)
    query_heads = queries.reshape(batch_count, seq_len, KVH, group_size, HD)
    grad_heads = out_grad.reshape(batch_count, seq_len, KVH, group_size, HD)
    key_heads = keys.reshape(batch_count, seq_len, KVH, HD)
    value_heads = values.reshape(batch_count, seq_len, KVH, HD)
    scores = (
        jnp.einsum("bqhgd,bkhd->bhgqk", query_heads, key_heads, preferred_element_type=jnp.float32)
        * scaling
    )
    position = jnp.arange(seq_len)
    causal = position[None, :] <= position[:, None]
    allowed = causal[None] & (segments[:, :, None] == segments[:, None, :])
    scores = jnp.where(allowed[:, None, None], scores, -1e30)
    highest = jnp.max(scores, axis=-1, keepdims=True)
    weights = jnp.exp(scores - highest)
    probabilities = weights / jnp.sum(weights, axis=-1, keepdims=True)
    probs_low = probabilities.astype(jnp.bfloat16)
    value_grad = jnp.einsum(
        "bhgqk,bqhgd->bkhd", probs_low, grad_heads, preferred_element_type=jnp.float32
    )
    prob_grad = jnp.einsum(
        "bqhgd,bkhd->bhgqk", grad_heads, value_heads, preferred_element_type=jnp.float32
    )
    row_dot = jnp.sum(probabilities * prob_grad, axis=-1, keepdims=True)
    score_grad = (probabilities * (prob_grad - row_dot) * scaling).astype(jnp.bfloat16)
    key_grad = jnp.einsum(
        "bhgqk,bqhgd->bkhd", score_grad, query_heads, preferred_element_type=jnp.float32
    )
    key_low = key_grad.astype(jnp.bfloat16).reshape(batch_count, seq_len, KVH * HD)
    value_low = value_grad.astype(jnp.bfloat16).reshape(batch_count, seq_len, KVH * HD)
    return jnp.concatenate([key_low, value_low], axis=-1)


def dp_reduce_scatter(partial, replicas, me):
    rows = partial.shape[0] // replicas
    total = lax.dynamic_slice_in_dim(partial, me * rows, rows, axis=0)
    for k in range(1, replicas):
        dest = (me + k) % replicas
        block = lax.dynamic_slice_in_dim(partial, dest * rows, rows, axis=0)
        total = total + lax.ppermute(
            block, "dp", [(d, (d + k) % replicas) for d in range(replicas)]
        )
    return total


def dp_all_gather(block, replicas, me):
    parts = [block]
    for k in range(1, replicas):
        parts.append(lax.ppermute(block, "dp", [(d, (d + k) % replicas) for d in range(replicas)]))
    order = (me - jnp.arange(replicas, dtype=jnp.int32)) % replicas
    gathered = jnp.take(jnp.stack(parts), order, axis=0)
    return gathered.reshape(replicas * block.shape[0], *block.shape[1:])


def local(parked, slot_order, segment_ids, queries, out_grad, norm_gain, kv_weight):
    sections = lax.axis_size("pipe")
    replicas = lax.axis_size("dp")
    me = lax.axis_index("dp")
    stored = parked[0]
    micro_count, seq_len, feature_count = stored.shape
    width = feature_count // replicas
    axes = ("pipe", "dp")
    own_order = slot_order[0, 0]
    next_order = lax.ppermute(own_order, "pipe", [(s, s - 1) for s in range(1, sections)])

    gain_full = norm_gain[0].astype(jnp.float32)
    gain_local = lax.dynamic_slice_in_dim(gain_full, me * width, width)
    local_weight = kv_weight[0]
    replica_ids = jnp.arange(replicas, dtype=jnp.int32)
    source_k = (me - replica_ids) % replicas

    def send_slot(slot):
        tokens = stored[slot]
        parts = []
        for k in range(replicas):
            col = (me + k) % replicas
            parts.append(lax.dynamic_slice_in_dim(tokens, col * width, width, axis=1))
        return parts

    def move_slot(parts):
        received = []
        for k in range(replicas):
            pairs = [
                (s * replicas + d, (sections - 1 - s) * replicas + (d + k) % replicas)
                for s in range(sections)
                for d in range(replicas)
            ]
            received.append(lax.ppermute(parts[k], axes, pairs))
        return received

    received = [move_slot(send_slot(0))]
    later = send_slot(1)
    received[0], later = lax.optimization_barrier((received[0], later))
    received.append(move_slot(later))

    def work_front(got):
        blocks = jnp.stack(got)
        x_cols = jnp.take(blocks, source_k, axis=0).reshape(replicas * seq_len, width)
        x_wide = x_cols.astype(jnp.float32)
        square_part = jnp.sum(x_wide * x_wide, axis=-1)
        square_sum = jnp.sum(dp_all_gather(square_part, replicas, me).reshape(replicas, -1), axis=0)
        inverse = lax.rsqrt(square_sum / feature_count + EPSILON)
        scale_col = inverse[:, None]
        normed = (x_wide * scale_col * gain_local).astype(jnp.bfloat16)
        partial = jnp.dot(normed, local_weight, preferred_element_type=jnp.float32)
        return partial, (x_wide, scale_col, normed)

    def work_mid(slot, partial):
        projected = dp_reduce_scatter(partial, replicas, me)
        projected_low = projected.astype(jnp.bfloat16)[None]
        head_span = projected_low.shape[-1] // 2
        micro = jnp.argmax(own_order == slot).astype(jnp.int32)
        kv_grads = attention_grads(
            lax.dynamic_slice_in_dim(queries[0], micro, 1, axis=0),
            lax.dynamic_slice_in_dim(out_grad[0], micro, 1, axis=0),
            projected_low[..., :head_span],
            projected_low[..., head_span:],
            lax.dynamic_slice_in_dim(segment_ids[0], micro, 1, axis=0),
        )
        kv_grads = kv_grads.reshape(seq_len, -1)
        return kv_grads

    def work_back(all_kv_grads, x_wide, scale_col):
        normed_grad = lax.dot_general(
            all_kv_grads, local_weight, (((1,), (1,)), ((), ())), preferred_element_type=jnp.float32
        )
        scaled_grad = normed_grad * gain_local
        inner_part = jnp.sum(scaled_grad * x_wide, axis=-1)
        inner_sum = jnp.sum(dp_all_gather(inner_part, replicas, me).reshape(replicas, -1), axis=0)
        inner_mean = inner_sum / feature_count
        input_grad = (
            scale_col * scaled_grad - x_wide * scale_col**3 * inner_mean[:, None]
        ).astype(jnp.bfloat16)
        gain_part = jnp.sum(normed_grad * x_wide * scale_col, axis=0)
        return input_grad, gain_part

    def weight_part_of(all_kv_grads, kept):
        return lax.dot_general(
            kept[2], all_kv_grads, (((0,), (0,)), ((), ())), preferred_element_type=jnp.float32
        )

    def piece_rows(value, piece, pieces):
        shaped = value.reshape(replicas, seq_len, *value.shape[1:])
        rows = seq_len // pieces
        return shaped[:, piece * rows:(piece + 1) * rows].reshape(replicas * rows, *value.shape[1:])

    def send_back(slot, input_grad, upstream, piece=0):
        micro = jnp.argmax(next_order == slot).astype(jnp.int32)
        rows = input_grad.shape[0] // replicas
        for k in range(replicas):
            pairs = [
                (s * replicas + d, (s - 1) * replicas + (d + k) % replicas)
                for s in range(1, sections)
                for d in range(replicas)
            ]
            dest = (me + k) % replicas
            block = lax.dynamic_slice_in_dim(input_grad, dest * rows, rows, axis=0)
            got_back = lax.ppermute(block, axes, pairs)
            upstream = lax.dynamic_update_slice(
                upstream, got_back[None], (micro, piece * rows, ((me - k) % replicas) * width)
            )
        return upstream

    partial0, kept0 = work_front(received[0])
    kv0 = work_mid(0, partial0)
    received[1], (kv0, kept0) = lax.optimization_barrier((received[1], (kv0, kept0)))
    partial1, kept1 = work_front(received[1])
    all_kv0 = dp_all_gather(kv0, replicas, me)
    all_kv0, partial1 = lax.optimization_barrier((all_kv0, partial1))
    kv1 = work_mid(1, partial1)
    grad0, gain_acc = work_back(all_kv0, kept0[0], kept0[1])
    weight_acc = weight_part_of(all_kv0, kept0)
    kv1, grad0 = lax.optimization_barrier((kv1, grad0))
    upstream = jnp.zeros((micro_count, seq_len, feature_count), jnp.bfloat16)
    upstream = send_back(0, grad0, upstream)
    all_kv1 = dp_all_gather(kv1, replicas, me)
    pieces = 2
    inputs = [
        tuple(piece_rows(v, h, pieces) for v in (all_kv1, kept1[0], kept1[1]))
        for h in range(pieces)
    ]
    for h in range(pieces):
        grad1, gain_part = work_back(*inputs[h])
        if h + 1 < pieces:
            inputs[h + 1], grad1 = lax.optimization_barrier((inputs[h + 1], grad1))
        gain_acc = gain_acc + gain_part
        upstream = send_back(1, grad1, upstream, piece=h)
    weight_acc = weight_acc + weight_part_of(all_kv1, kept1)

    weight_grad = weight_acc.astype(jnp.bfloat16)
    gain_grad = lax.all_gather(gain_acc, "dp", axis=0, tiled=True)
    return (upstream[None], weight_grad[None], gain_grad[None])


def solution(mesh):
    return jax.shard_map(
        local,
        mesh=mesh,
        in_specs=(
            P("pipe", "dp", None, None),
            P("pipe", "dp", None),
            P("pipe", "dp", None),
            P("pipe", "dp", None, None),
            P("pipe", "dp", None, None),
            P("pipe", None),
            P("pipe", "dp", None),
        ),
        out_specs=(P("pipe", "dp", None, None), P("pipe", "dp", None), P("pipe", None)),
        check_vma=False,
    )
```
